512 devices in a mesh: dp: 8 (over x_hi, y), tm: 64 (over x_lo, z, core).
Axes of the slice: x: 4 (x_hi: 2, x_lo: 2; x = x_hi * 2 + x_lo), y: 4, z: 16, core: 2. Of those that a mesh axis runs over, the one named last changes fastest.
Arguments:
- signal: bfloat16 [8, 65536, 256], P('dp', 'tm'), may hold values from -6 to 6
- cotangent: bfloat16 [8, 65536, 256], P('dp', 'tm'), may hold values from -6 to 6
- first_history_weight: bfloat16 [256, 512], replicated, may hold values from -0.25 to 0.25
- first_current_weight: bfloat16 [256, 512], replicated, may hold values from -0.25 to 0.25
- first_residual_weight: bfloat16 [256, 256], replicated, may hold values from -0.375 to 0.375
- second_history_weight: bfloat16 [256, 512], replicated, may hold values from -0.25 to 0.25
- second_current_weight: bfloat16 [256, 512], replicated, may hold values from -0.25 to 0.25
- second_residual_weight: bfloat16 [256, 256], replicated, may hold values from -0.375 to 0.375
Outputs:
- grad_signal: bfloat16 [8, 65536, 256], P('dp', 'tm')
- grad_past_one: bfloat16 [256, 512], replicated
- grad_now_one: bfloat16 [256, 512], replicated
- grad_mix_one: bfloat16 [256, 256], replicated
- grad_past_two: bfloat16 [256, 512], replicated
- grad_now_two: bfloat16 [256, 512], replicated
- grad_mix_two: bfloat16 [256, 256], replicated
The draws below stay inside these ranges and needn't reach their ends.
All inputs are finite; a program needn't handle non-finite values.
Results may differ from the reference program's by a relative error of at most 0.0068.
Values may be sent and summed in bfloat16 or wider, within the bound.
No kernel may reach another device: no remote copies, remote signals or barrier semaphores. Data moves between devices by JAX's collectives and lax.ppermute only.
A program may use at most 64 MiB of HBM per device.

```python
import math
import jax
import jax.numpy as jnp
from jax import lax

RES = 256
GATE = 512
FIRST_DILATION = 512
SECOND_DILATION = 8192
BATCH = 8
LENGTH = 65536


def steps_of(own_key, extent, shards, smallest, high):
    level = 1.0
    for axis_at, blocks in shards:
        steps = jax.random.uniform(jax.random.fold_in(jax.random.fold_in(own_key, 6), axis_at), (blocks,), jnp.float32, smallest / len(shards), high / len(shards))
        level = level * jnp.repeat(jnp.exp(steps), extent[axis_at] // blocks).reshape((-1,) + (1,) * (len(extent) - 1 - axis_at))
    return level


def noise(key, dims, width, limit, cuts=(), kind=jnp.bfloat16):
    array = width * jax.random.normal(key, dims, jnp.float32)
    if cuts:
        array = array * steps_of(key, dims, cuts, -0.22, 0.18)
    return jnp.clip(array, -limit, limit).astype(kind)


def setup_inputs(seed: int = 0) -> dict:
    keys = jax.random.split(jax.random.key(seed), 9)
    return {
        "signal": noise(keys[0], (BATCH, LENGTH, RES), 1.0, 6.0, ((0, 8), (1, 64))),
        "cotangent": noise(keys[1], (BATCH, LENGTH, RES), 1.0, 6.0, ((0, 8), (1, 64))),
        "first_history_weight": noise(keys[2], (RES, GATE), (2 * RES) ** -0.5, 0.25),
        "first_current_weight": noise(keys[3], (RES, GATE), (2 * RES) ** -0.5, 0.25),
        "first_residual_weight": noise(keys[4], (GATE // 2, RES), (GATE // 2) ** -0.5, 0.375),
        "second_history_weight": noise(keys[5], (RES, GATE), (2 * RES) ** -0.5, 0.25),
        "second_current_weight": noise(keys[6], (RES, GATE), (2 * RES) ** -0.5, 0.25),
        "second_residual_weight": noise(keys[7], (GATE // 2, RES), (GATE // 2) ** -0.5, 0.375),
    }


def gated_layer_forward(input_traces, tap_past, tap_now, mixing, dilation):
    zero_rows = jnp.zeros((dilation, input_traces.shape[1]), input_traces.dtype)
    past_rows = jnp.concatenate([zero_rows, input_traces[:-dilation]], axis=0)
    pre_act = jnp.dot(past_rows, tap_past, preferred_element_type=jnp.float32) + jnp.dot(input_traces, tap_now, preferred_element_type=jnp.float32)
    half_width = pre_act.shape[1] // 2
    filter_part = jnp.tanh(pre_act[:, :half_width])
    gate_part = jax.nn.sigmoid(pre_act[:, half_width:])
    hidden = (filter_part * gate_part).astype(jnp.bfloat16)
    output = (input_traces.astype(jnp.float32) + jnp.dot(hidden, mixing, preferred_element_type=jnp.float32)).astype(jnp.bfloat16)
    return (past_rows, filter_part, gate_part, hidden, output)

def gated_layer_backward(input_traces, saved, incoming_gradient, tap_past, tap_now, mixing, dilation):
    past_rows, filter_part, gate_part, hidden, output = saved
    hidden_grad = jnp.dot(incoming_gradient, mixing.T, preferred_element_type=jnp.float32)
    filter_grad = hidden_grad * gate_part * (1.0 - filter_part * filter_part)
    gate_grad = hidden_grad * filter_part * gate_part * (1.0 - gate_part)
    pre_grad = jnp.concatenate([filter_grad, gate_grad], axis=1).astype(jnp.bfloat16)
    past_term = jnp.dot(past_rows.T, pre_grad, preferred_element_type=jnp.float32)
    now_term = jnp.dot(input_traces.T, pre_grad, preferred_element_type=jnp.float32)
    mix_term = jnp.dot(hidden.T, incoming_gradient, preferred_element_type=jnp.float32)
    ahead_rows = jnp.dot(pre_grad, tap_past.T, preferred_element_type=jnp.float32).astype(jnp.bfloat16)
    zero_rows = jnp.zeros((dilation, ahead_rows.shape[1]), ahead_rows.dtype)
    trailing_later_rows = jnp.concatenate([ahead_rows[dilation:], zero_rows], axis=0)
    input_grad = (incoming_gradient.astype(jnp.float32) + jnp.dot(pre_grad, tap_now.T, preferred_element_type=jnp.float32) + trailing_later_rows.astype(jnp.float32)).astype(jnp.bfloat16)
    return (input_grad, (past_term, now_term, mix_term))

def finish_term(stacked, scale_factor):
    return (lax.optimization_barrier(jnp.sum(stacked, axis=0)) * scale_factor).astype(jnp.bfloat16)

def reference(signal, cotangent, first_history_weight, first_current_weight, first_residual_weight, second_history_weight, second_current_weight, second_residual_weight):

    def one_sequence(pair):
        input_traces, incoming_gradient = pair
        first_layer_stash = gated_layer_forward(input_traces, first_history_weight, first_current_weight, first_residual_weight, FIRST_DILATION)
        hidden_activation = first_layer_stash[4]
        second_layer_stash = gated_layer_forward(hidden_activation, second_history_weight, second_current_weight, second_residual_weight, SECOND_DILATION)
        hidden_gradient, second_layer_terms = gated_layer_backward(hidden_activation, second_layer_stash, incoming_gradient, second_history_weight, second_current_weight, second_residual_weight, SECOND_DILATION)
        input_gradient, first_layer_terms = gated_layer_backward(input_traces, first_layer_stash, hidden_gradient, first_history_weight, first_current_weight, first_residual_weight, FIRST_DILATION)
        return (input_gradient, first_layer_terms, second_layer_terms)
    grad_signal, first_layer_terms, second_layer_terms = lax.map(one_sequence, (signal, cotangent))
    scale_factor = 1.0 / math.sqrt(BATCH * LENGTH)
    return (grad_signal, finish_term(first_layer_terms[0], scale_factor), finish_term(first_layer_terms[1], scale_factor), finish_term(first_layer_terms[2], scale_factor), finish_term(second_layer_terms[0], scale_factor), finish_term(second_layer_terms[1], scale_factor), finish_term(second_layer_terms[2], scale_factor))
```

```python
import math

import jax
import jax.numpy as jnp
from jax import lax
from jax.sharding import PartitionSpec as P

FIRST_DILATION = 512
SECOND_DILATION = 8192


def shifted(value, axis, steps):
    count = lax.axis_size(axis)
    leading, last = (max(0, -steps), min(count, count - steps))
    return lax.ppermute(value, axis, [(source, source + steps) for source in range(leading, last)])


def forward_layer(input_traces, past_rows, tap_past, tap_now, mixing):
    channels = input_traces.shape[-1]
    flat_now = input_traces.reshape(-1, channels)
    flat_past = past_rows.reshape(-1, channels)
    pre_act = jnp.dot(flat_past, tap_past, preferred_element_type=jnp.float32) + jnp.dot(
        flat_now, tap_now, preferred_element_type=jnp.float32
    )
    half_width = pre_act.shape[1] // 2
    filter_part = jnp.tanh(pre_act[:, :half_width])
    gate_part = jax.nn.sigmoid(pre_act[:, half_width:])
    hidden = (filter_part * gate_part).astype(jnp.bfloat16)
    output = (
        flat_now.astype(jnp.float32) + jnp.dot(hidden, mixing, preferred_element_type=jnp.float32)
    ).astype(jnp.bfloat16)
    return (filter_part, gate_part, hidden, output.reshape(input_traces.shape))


def backward_layer(input_traces, past_rows, saved, incoming_gradient, tap_past, tap_now, mixing):
    filter_part, gate_part, hidden, output = saved
    channels = input_traces.shape[-1]
    flat_now = input_traces.reshape(-1, channels)
    flat_past = past_rows.reshape(-1, channels)
    flat_up = incoming_gradient.reshape(-1, channels)
    hidden_grad = jnp.dot(flat_up, mixing.T, preferred_element_type=jnp.float32)
    filter_grad = hidden_grad * gate_part * (1.0 - filter_part * filter_part)
    gate_grad = hidden_grad * filter_part * gate_part * (1.0 - gate_part)
    pre_grad = jnp.concatenate([filter_grad, gate_grad], axis=1).astype(jnp.bfloat16)
    past_term = jnp.einsum("rc,rg->cg", flat_past, pre_grad, preferred_element_type=jnp.float32)
    now_term = jnp.einsum("rc,rg->cg", flat_now, pre_grad, preferred_element_type=jnp.float32)
    mix_term = jnp.einsum("rh,rc->hc", hidden, flat_up, preferred_element_type=jnp.float32)
    ahead_rows = (
        jnp.dot(pre_grad, tap_past.T, preferred_element_type=jnp.float32)
        .astype(jnp.bfloat16)
        .reshape(input_traces.shape)
    )
    local_grad = (
        flat_up.astype(jnp.float32)
        + jnp.dot(pre_grad, tap_now.T, preferred_element_type=jnp.float32)
    ).reshape(input_traces.shape)
    return (local_grad, ahead_rows, (past_term, now_term, mix_term))


REDUCE_STEPS = (("tm", 1), ("tm", 32), ("tm", 2), ("dp", 1), ("dp", 4), ("tm", 4), ("dp", 2), ("tm", 8), ("tm", 16))


def exchange(value, axis, mask):
    count = lax.axis_size(axis)
    return lax.ppermute(value, axis, [(source, source ^ mask) for source in range(count)])


def halving_sum(flat):
    for axis, mask in REDUCE_STEPS:
        half = flat.shape[0] // 2
        upper = (lax.axis_index(axis) & mask) != 0
        first, second = flat[:half], flat[half:]
        kept = jnp.where(upper, second, first)
        sent = jnp.where(upper, first, second)
        flat = kept + exchange(sent, axis, mask)
    for axis, mask in reversed(REDUCE_STEPS):
        upper = (lax.axis_index(axis) & mask) != 0
        other = exchange(flat, axis, mask)
        flat = jnp.where(upper, jnp.concatenate([other, flat]), jnp.concatenate([flat, other]))
    return flat


def reduce_grads(term_list, scale_factor):
    shapes = [member.shape for member in term_list]
    flat = jnp.concatenate([member.reshape(-1, 128) for member in term_list])
    summed = halving_sum(flat)
    out, start = [], 0
    for shape in shapes:
        rows = shape[0] * shape[1] // 128
        out.append((summed[start:start + rows].reshape(shape) * scale_factor).astype(jnp.bfloat16))
        start += rows
    return tuple(out)


def body(
    signal,
    cotangent,
    first_history_weight,
    first_current_weight,
    first_residual_weight,
    second_history_weight,
    second_current_weight,
    second_residual_weight,
):
    seq_count, number_of_steps, channels = signal.shape
    rows_all = seq_count * lax.axis_size("dp") * number_of_steps * lax.axis_size("tm")
    scale_factor = 1.0 / math.sqrt(rows_all)
    final_rows = signal[:, number_of_steps - FIRST_DILATION :, :]
    received_rows = shifted(final_rows, "tm", 1)
    first_history_rows = jnp.concatenate(
        [received_rows, signal[:, : number_of_steps - FIRST_DILATION, :]], axis=1
    )
    first_layer_stash = forward_layer(
        signal,
        first_history_rows,
        first_history_weight,
        first_current_weight,
        first_residual_weight,
    )
    hidden_activation = first_layer_stash[3]
    distant_offsets = SECOND_DILATION // number_of_steps
    past_two = shifted(hidden_activation, "tm", distant_offsets)
    second_layer_stash = forward_layer(
        hidden_activation,
        past_two,
        second_history_weight,
        second_current_weight,
        second_residual_weight,
    )
    local_two, ahead_two, second_layer_terms = backward_layer(
        hidden_activation,
        past_two,
        second_layer_stash,
        cotangent,
        second_history_weight,
        second_current_weight,
        second_residual_weight,
    )
    arrived_back = shifted(ahead_two, "tm", -distant_offsets)
    hidden_gradient = (local_two + arrived_back.astype(jnp.float32)).astype(jnp.bfloat16)
    local_one, forward_rows_first, first_layer_terms = backward_layer(
        signal,
        first_history_rows,
        first_layer_stash,
        hidden_gradient,
        first_history_weight,
        first_current_weight,
        first_residual_weight,
    )
    leading_rows = forward_rows_first[:, :FIRST_DILATION, :]
    received_head_rows = shifted(leading_rows, "tm", -1)
    trailing_later_rows = jnp.concatenate(
        [forward_rows_first[:, FIRST_DILATION:, :], received_head_rows], axis=1
    )
    grad_signal = (local_one + trailing_later_rows.astype(jnp.float32)).astype(jnp.bfloat16)
    reduced = reduce_grads(tuple(first_layer_terms) + tuple(second_layer_terms), scale_factor)
    reduced_one, reduced_two = reduced[:3], reduced[3:]
    return (
        grad_signal,
        reduced_one[0],
        reduced_one[1],
        reduced_one[2],
        reduced_two[0],
        reduced_two[1],
        reduced_two[2],
    )


def solution(mesh):
    in_specs = (P("dp", "tm", None), P("dp", "tm", None), P(), P(), P(), P(), P(), P())
    out_specs = (P("dp", "tm", None), P(), P(), P(), P(), P(), P())
    return jax.shard_map(body, mesh=mesh, in_specs=in_specs, out_specs=out_specs, check_vma=False)
```

```python
import math

import jax
import jax.numpy as jnp
from jax import lax
from jax.sharding import PartitionSpec as P

FIRST_DILATION = 512
SECOND_DILATION = 8192


def shifted(value, axis, steps):
    count = lax.axis_size(axis)
    leading, last = (max(0, -steps), min(count, count - steps))
    return lax.ppermute(value, axis, [(source, source + steps) for source in range(leading, last)])


def forward_layer(input_traces, past_rows, tap_past, tap_now, mixing):
    channels = input_traces.shape[-1]
    flat_now = input_traces.reshape(-1, channels)
    flat_past = past_rows.reshape(-1, channels)
    pre_act = jnp.dot(flat_past, tap_past, preferred_element_type=jnp.float32) + jnp.dot(
        flat_now, tap_now, preferred_element_type=jnp.float32
    )
    half_width = pre_act.shape[1] // 2
    filter_part = jnp.tanh(pre_act[:, :half_width])
    gate_part = jax.nn.sigmoid(pre_act[:, half_width:])
    hidden = (filter_part * gate_part).astype(jnp.bfloat16)
    output = (
        flat_now.astype(jnp.float32) + jnp.dot(hidden, mixing, preferred_element_type=jnp.float32)
    ).astype(jnp.bfloat16)
    return (filter_part, gate_part, hidden, output.reshape(input_traces.shape))


def backward_layer(input_traces, past_rows, saved, incoming_gradient, tap_past, tap_now, mixing):
    filter_part, gate_part, hidden, output = saved
    channels = input_traces.shape[-1]
    flat_now = input_traces.reshape(-1, channels)
    flat_past = past_rows.reshape(-1, channels)
    flat_up = incoming_gradient.reshape(-1, channels)
    hidden_grad = jnp.dot(flat_up, mixing.T, preferred_element_type=jnp.float32)
    filter_grad = hidden_grad * gate_part * (1.0 - filter_part * filter_part)
    gate_grad = hidden_grad * filter_part * gate_part * (1.0 - gate_part)
    pre_grad = jnp.concatenate([filter_grad, gate_grad], axis=1).astype(jnp.bfloat16)
    past_term = jnp.einsum("rc,rg->cg", flat_past, pre_grad, preferred_element_type=jnp.float32)
    now_term = jnp.einsum("rc,rg->cg", flat_now, pre_grad, preferred_element_type=jnp.float32)
    mix_term = jnp.einsum("rh,rc->hc", hidden, flat_up, preferred_element_type=jnp.float32)
    ahead_rows = (
        jnp.dot(pre_grad, tap_past.T, preferred_element_type=jnp.float32)
        .astype(jnp.bfloat16)
        .reshape(input_traces.shape)
    )
    local_grad = (
        flat_up.astype(jnp.float32)
        + jnp.dot(pre_grad, tap_now.T, preferred_element_type=jnp.float32)
    ).reshape(input_traces.shape)
    return (local_grad, ahead_rows, (past_term, now_term, mix_term))


ROUNDS = ((1,), (32, 64), (2, 4), (256, 128), (8, 16))
AXES = ("dp", "tm")


def spread(code, bits):
    return sum(bit for place, bit in enumerate(bits) if code >> place & 1)


def position(bits):
    index = lax.axis_index(AXES)
    return sum(((index // bit) % 2) << place for place, bit in enumerate(bits))


def partner_pairs(mask):
    count = lax.axis_size(AXES)
    return [(source, source ^ mask) for source in range(count)]


def scatter_round(flat, bits):
    ways = 1 << len(bits)
    me = position(bits)
    pieces = flat.reshape((ways, flat.shape[0] // ways) + flat.shape[1:])
    total = lax.dynamic_index_in_dim(pieces, me, keepdims=False)
    for code in range(1, ways):
        sent = lax.dynamic_index_in_dim(pieces, me ^ code, keepdims=False)
        total = total + lax.ppermute(sent, AXES, partner_pairs(spread(code, bits)))
    return total


def gather_round(piece, bits):
    ways = 1 << len(bits)
    me = position(bits)
    arrived = [piece] + [lax.ppermute(piece, AXES, partner_pairs(spread(code, bits))) for code in range(1, ways)]
    stacked = jnp.stack(arrived)
    order = jnp.arange(ways) ^ me
    return jnp.take(stacked, order, axis=0).reshape((-1,) + piece.shape[1:])


def reduce_grads(term_list, scale_factor):
    shapes = [member.shape for member in term_list]
    flat = jnp.concatenate([member.reshape(-1, 128) for member in term_list])
    for bits in ROUNDS:
        flat = scatter_round(flat, bits)
    flat = (flat * scale_factor).astype(jnp.bfloat16)
    for bits in reversed(ROUNDS):
        flat = gather_round(flat, bits)
    out, start = [], 0
    for shape in shapes:
        rows = shape[0] * shape[1] // 128
        out.append(flat[start:start + rows].reshape(shape))
        start += rows
    return tuple(out)


def body(
    signal,
    cotangent,
    first_history_weight,
    first_current_weight,
    first_residual_weight,
    second_history_weight,
    second_current_weight,
    second_residual_weight,
):
    seq_count, number_of_steps, channels = signal.shape
    rows_all = seq_count * lax.axis_size("dp") * number_of_steps * lax.axis_size("tm")
    scale_factor = 1.0 / math.sqrt(rows_all)
    final_rows = signal[:, number_of_steps - FIRST_DILATION :, :]
    received_rows = shifted(final_rows, "tm", 1)
    first_history_rows = jnp.concatenate(
        [received_rows, signal[:, : number_of_steps - FIRST_DILATION, :]], axis=1
    )
    first_layer_stash = forward_layer(
        signal,
        first_history_rows,
        first_history_weight,
        first_current_weight,
        first_residual_weight,
    )
    hidden_activation = first_layer_stash[3]
    distant_offsets = SECOND_DILATION // number_of_steps
    past_two = shifted(hidden_activation, "tm", distant_offsets)
    second_layer_stash = forward_layer(
        hidden_activation,
        past_two,
        second_history_weight,
        second_current_weight,
        second_residual_weight,
    )
    local_two, ahead_two, second_layer_terms = backward_layer(
        hidden_activation,
        past_two,
        second_layer_stash,
        cotangent,
        second_history_weight,
        second_current_weight,
        second_residual_weight,
    )
    arrived_back = shifted(ahead_two, "tm", -distant_offsets)
    hidden_gradient = (local_two + arrived_back.astype(jnp.float32)).astype(jnp.bfloat16)
    local_one, forward_rows_first, first_layer_terms = backward_layer(
        signal,
        first_history_rows,
        first_layer_stash,
        hidden_gradient,
        first_history_weight,
        first_current_weight,
        first_residual_weight,
    )
    leading_rows = forward_rows_first[:, :FIRST_DILATION, :]
    received_head_rows = shifted(leading_rows, "tm", -1)
    trailing_later_rows = jnp.concatenate(
        [forward_rows_first[:, FIRST_DILATION:, :], received_head_rows], axis=1
    )
    grad_signal = (local_one + trailing_later_rows.astype(jnp.float32)).astype(jnp.bfloat16)
    reduced = reduce_grads(tuple(first_layer_terms) + tuple(second_layer_terms), scale_factor)
    reduced_one, reduced_two = reduced[:3], reduced[3:]
    return (
        grad_signal,
        reduced_one[0],
        reduced_one[1],
        reduced_one[2],
        reduced_two[0],
        reduced_two[1],
        reduced_two[2],
    )


def solution(mesh):
    in_specs = (P("dp", "tm", None), P("dp", "tm", None), P(), P(), P(), P(), P(), P())
    out_specs = (P("dp", "tm", None), P(), P(), P(), P(), P(), P())
    return jax.shard_map(body, mesh=mesh, in_specs=in_specs, out_specs=out_specs, check_vma=False)
```

```python
import math

import jax
import jax.numpy as jnp
from jax import lax
from jax.sharding import PartitionSpec as P

FIRST_DILATION = 512
SECOND_DILATION = 8192


def shifted(value, axis, steps):
    count = lax.axis_size(axis)
    leading, last = (max(0, -steps), min(count, count - steps))
    return lax.ppermute(value, axis, [(source, source + steps) for source in range(leading, last)])


def forward_layer(input_traces, past_rows, tap_past, tap_now, mixing):
    channels = input_traces.shape[-1]
    flat_now = input_traces.reshape(-1, channels)
    flat_past = past_rows.reshape(-1, channels)
    pre_act = jnp.dot(flat_past, tap_past, preferred_element_type=jnp.float32) + jnp.dot(
        flat_now, tap_now, preferred_element_type=jnp.float32
    )
    half_width = pre_act.shape[1] // 2
    filter_part = jnp.tanh(pre_act[:, :half_width])
    gate_part = jax.nn.sigmoid(pre_act[:, half_width:])
    hidden = (filter_part * gate_part).astype(jnp.bfloat16)
    output = (
        flat_now.astype(jnp.float32) + jnp.dot(hidden, mixing, preferred_element_type=jnp.float32)
    ).astype(jnp.bfloat16)
    return (filter_part, gate_part, hidden, output.reshape(input_traces.shape))


def backward_layer(input_traces, past_rows, saved, incoming_gradient, tap_past, tap_now, mixing):
    filter_part, gate_part, hidden, output = saved
    channels = input_traces.shape[-1]
    flat_now = input_traces.reshape(-1, channels)
    flat_past = past_rows.reshape(-1, channels)
    flat_up = incoming_gradient.reshape(-1, channels)
    hidden_grad = jnp.dot(flat_up, mixing.T, preferred_element_type=jnp.float32)
    filter_grad = hidden_grad * gate_part * (1.0 - filter_part * filter_part)
    gate_grad = hidden_grad * filter_part * gate_part * (1.0 - gate_part)
    pre_grad = jnp.concatenate([filter_grad, gate_grad], axis=1).astype(jnp.bfloat16)
    past_term = jnp.einsum("rc,rg->cg", flat_past, pre_grad, preferred_element_type=jnp.float32)
    now_term = jnp.einsum("rc,rg->cg", flat_now, pre_grad, preferred_element_type=jnp.float32)
    mix_term = jnp.einsum("rh,rc->hc", hidden, flat_up, preferred_element_type=jnp.float32)
    ahead_rows = (
        jnp.dot(pre_grad, tap_past.T, preferred_element_type=jnp.float32)
        .astype(jnp.bfloat16)
        .reshape(input_traces.shape)
    )
    local_grad = (
        flat_up.astype(jnp.float32)
        + jnp.dot(pre_grad, tap_now.T, preferred_element_type=jnp.float32)
    ).reshape(input_traces.shape)
    return (local_grad, ahead_rows, (past_term, now_term, mix_term))


HALVING_STEPS = (("tm", 1), ("tm", 32), ("dp", 1), ("tm", 2), ("dp", 4), ("dp", 2))
BUTTERFLY_STEPS = (("tm", 4), ("tm", 8), ("tm", 16))


def exchange(value, axis, mask):
    count = lax.axis_size(axis)
    return lax.ppermute(value, axis, [(source, source ^ mask) for source in range(count)])


def reduce_grads(term_list, scale_factor):
    shapes = [member.shape for member in term_list]
    flat = jnp.concatenate([member.reshape(-1, 128) for member in term_list])
    for axis, mask in HALVING_STEPS:
        half = flat.shape[0] // 2
        upper = (lax.axis_index(axis) & mask) != 0
        first, second = flat[:half], flat[half:]
        kept = jnp.where(upper, second, first)
        sent = jnp.where(upper, first, second)
        flat = kept + exchange(sent, axis, mask)
    for axis, mask in BUTTERFLY_STEPS:
        flat = flat + exchange(flat, axis, mask)
    flat = (flat * scale_factor).astype(jnp.bfloat16)
    for axis, mask in reversed(HALVING_STEPS):
        upper = (lax.axis_index(axis) & mask) != 0
        other = exchange(flat, axis, mask)
        flat = jnp.where(upper, jnp.concatenate([other, flat]), jnp.concatenate([flat, other]))
    out, start = [], 0
    for shape in shapes:
        rows = shape[0] * shape[1] // 128
        out.append(flat[start:start + rows].reshape(shape))
        start += rows
    return tuple(out)


def body(
    signal,
    cotangent,
    first_history_weight,
    first_current_weight,
    first_residual_weight,
    second_history_weight,
    second_current_weight,
    second_residual_weight,
):
    seq_count, number_of_steps, channels = signal.shape
    rows_all = seq_count * lax.axis_size("dp") * number_of_steps * lax.axis_size("tm")
    scale_factor = 1.0 / math.sqrt(rows_all)
    final_rows = signal[:, number_of_steps - FIRST_DILATION :, :]
    received_rows = shifted(final_rows, "tm", 1)
    first_history_rows = jnp.concatenate(
        [received_rows, signal[:, : number_of_steps - FIRST_DILATION, :]], axis=1
    )
    first_layer_stash = forward_layer(
        signal,
        first_history_rows,
        first_history_weight,
        first_current_weight,
        first_residual_weight,
    )
    hidden_activation = first_layer_stash[3]
    distant_offsets = SECOND_DILATION // number_of_steps
    past_two = shifted(hidden_activation, "tm", distant_offsets)
    second_layer_stash = forward_layer(
        hidden_activation,
        past_two,
        second_history_weight,
        second_current_weight,
        second_residual_weight,
    )
    local_two, ahead_two, second_layer_terms = backward_layer(
        hidden_activation,
        past_two,
        second_layer_stash,
        cotangent,
        second_history_weight,
        second_current_weight,
        second_residual_weight,
    )
    arrived_back = shifted(ahead_two, "tm", -distant_offsets)
    hidden_gradient = (local_two + arrived_back.astype(jnp.float32)).astype(jnp.bfloat16)
    local_one, forward_rows_first, first_layer_terms = backward_layer(
        signal,
        first_history_rows,
        first_layer_stash,
        hidden_gradient,
        first_history_weight,
        first_current_weight,
        first_residual_weight,
    )
    leading_rows = forward_rows_first[:, :FIRST_DILATION, :]
    received_head_rows = shifted(leading_rows, "tm", -1)
    trailing_later_rows = jnp.concatenate(
        [forward_rows_first[:, FIRST_DILATION:, :], received_head_rows], axis=1
    )
    grad_signal = (local_one + trailing_later_rows.astype(jnp.float32)).astype(jnp.bfloat16)
    reduced = reduce_grads(tuple(first_layer_terms) + tuple(second_layer_terms), scale_factor)
    reduced_one, reduced_two = reduced[:3], reduced[3:]
    return (
        grad_signal,
        reduced_one[0],
        reduced_one[1],
        reduced_one[2],
        reduced_two[0],
        reduced_two[1],
        reduced_two[2],
    )


def solution(mesh):
    in_specs = (P("dp", "tm", None), P("dp", "tm", None), P(), P(), P(), P(), P(), P())
    out_specs = (P("dp", "tm", None), P(), P(), P(), P(), P(), P())
    return jax.shard_map(body, mesh=mesh, in_specs=in_specs, out_specs=out_specs, check_vma=False)
```

```python
import math

import jax
import jax.numpy as jnp
from jax import lax
from jax.sharding import PartitionSpec as P

FIRST_DILATION = 512
SECOND_DILATION = 8192


def shifted(value, axis, steps):
    count = lax.axis_size(axis)
    leading, last = (max(0, -steps), min(count, count - steps))
    return lax.ppermute(value, axis, [(source, source + steps) for source in range(leading, last)])


def forward_layer(input_traces, past_rows, tap_past, tap_now, mixing):
    channels = input_traces.shape[-1]
    flat_now = input_traces.reshape(-1, channels)
    flat_past = past_rows.reshape(-1, channels)
    pre_act = jnp.dot(flat_past, tap_past, preferred_element_type=jnp.float32) + jnp.dot(
        flat_now, tap_now, preferred_element_type=jnp.float32
    )
    half_width = pre_act.shape[1] // 2
    filter_part = jnp.tanh(pre_act[:, :half_width])
    gate_part = jax.nn.sigmoid(pre_act[:, half_width:])
    hidden = (filter_part * gate_part).astype(jnp.bfloat16)
    output = (
        flat_now.astype(jnp.float32) + jnp.dot(hidden, mixing, preferred_element_type=jnp.float32)
    ).astype(jnp.bfloat16)
    return (filter_part, gate_part, hidden, output.reshape(input_traces.shape))


def backward_layer(input_traces, past_rows, saved, incoming_gradient, tap_past, tap_now, mixing):
    filter_part, gate_part, hidden, output = saved
    channels = input_traces.shape[-1]
    flat_now = input_traces.reshape(-1, channels)
    flat_past = past_rows.reshape(-1, channels)
    flat_up = incoming_gradient.reshape(-1, channels)
    hidden_grad = jnp.dot(flat_up, mixing.T, preferred_element_type=jnp.float32)
    filter_grad = hidden_grad * gate_part * (1.0 - filter_part * filter_part)
    gate_grad = hidden_grad * filter_part * gate_part * (1.0 - gate_part)
    pre_grad = jnp.concatenate([filter_grad, gate_grad], axis=1).astype(jnp.bfloat16)
    past_term = jnp.einsum("rc,rg->cg", flat_past, pre_grad, preferred_element_type=jnp.float32)
    now_term = jnp.einsum("rc,rg->cg", flat_now, pre_grad, preferred_element_type=jnp.float32)
    mix_term = jnp.einsum("rh,rc->hc", hidden, flat_up, preferred_element_type=jnp.float32)
    ahead_rows = (
        jnp.dot(pre_grad, tap_past.T, preferred_element_type=jnp.float32)
        .astype(jnp.bfloat16)
        .reshape(input_traces.shape)
    )
    local_grad = (
        flat_up.astype(jnp.float32)
        + jnp.dot(pre_grad, tap_now.T, preferred_element_type=jnp.float32)
    ).reshape(input_traces.shape)
    return (local_grad, ahead_rows, (past_term, now_term, mix_term))


HALVING_STEPS = (("tm", 1), ("tm", 32), ("dp", 1), ("tm", 2), ("dp", 4), ("dp", 2))
BUTTERFLY_STEPS = (("tm", 4), ("tm", 8), ("tm", 16))


def exchange(value, axis, mask):
    count = lax.axis_size(axis)
    return lax.ppermute(value, axis, [(source, source ^ mask) for source in range(count)])


def reduce_grads(term_list, scale_factor):
    shapes = [member.shape for member in term_list]
    flat = jnp.concatenate([member.reshape(-1, 128) for member in term_list])
    for axis, mask in HALVING_STEPS:
        half = flat.shape[0] // 2
        upper = (lax.axis_index(axis) & mask) != 0
        first, second = flat[:half], flat[half:]
        kept = jnp.where(upper, second, first)
        sent = jnp.where(upper, first, second)
        flat = kept + exchange(sent, axis, mask)
    for axis, mask in BUTTERFLY_STEPS:
        flat = flat + exchange(flat, axis, mask)
    flat = (flat * scale_factor).astype(jnp.bfloat16)
    for axis, mask in reversed(HALVING_STEPS):
        upper = (lax.axis_index(axis) & mask) != 0
        other = exchange(flat, axis, mask)
        flat = jnp.where(upper, jnp.concatenate([other, flat]), jnp.concatenate([flat, other]))
    out, start = [], 0
    for shape in shapes:
        rows = shape[0] * shape[1] // 128
        out.append(flat[start:start + rows].reshape(shape))
        start += rows
    return tuple(out)


def body(
    signal,
    cotangent,
    first_history_weight,
    first_current_weight,
    first_residual_weight,
    second_history_weight,
    second_current_weight,
    second_residual_weight,
):
    seq_count, number_of_steps, channels = signal.shape
    rows_all = seq_count * lax.axis_size("dp") * number_of_steps * lax.axis_size("tm")
    scale_factor = 1.0 / math.sqrt(rows_all)
    final_rows = signal[:, number_of_steps - FIRST_DILATION :, :]
    received_rows = shifted(final_rows, "tm", 1)
    first_history_rows = jnp.concatenate(
        [received_rows, signal[:, : number_of_steps - FIRST_DILATION, :]], axis=1
    )
    first_layer_stash = forward_layer(
        signal,
        first_history_rows,
        first_history_weight,
        first_current_weight,
        first_residual_weight,
    )
    hidden_activation = first_layer_stash[3]
    distant_offsets = SECOND_DILATION // number_of_steps
    chunk_rows = number_of_steps // 2
    local_parts, arrived_parts, term_parts, past_parts = [], [], [], []
    for chunk in range(2):
        rows = slice(chunk * chunk_rows, (chunk + 1) * chunk_rows)
        hidden_chunk = hidden_activation[:, rows, :]
        if chunk:
            hidden_chunk, _ = lax.optimization_barrier((hidden_chunk, past_parts[-1]))
        past_chunk = shifted(hidden_chunk, "tm", distant_offsets)
        past_parts.append(past_chunk)
        chunk_stash = forward_layer(
            hidden_chunk,
            past_chunk,
            second_history_weight,
            second_current_weight,
            second_residual_weight,
        )
        local_chunk, ahead_chunk, chunk_terms = backward_layer(
            hidden_chunk,
            past_chunk,
            chunk_stash,
            cotangent[:, rows, :],
            second_history_weight,
            second_current_weight,
            second_residual_weight,
        )
        local_parts.append(local_chunk)
        arrived_parts.append(shifted(ahead_chunk, "tm", -distant_offsets))
        term_parts.append(chunk_terms)
    local_two = jnp.concatenate(local_parts, axis=1)
    arrived_back = jnp.concatenate(arrived_parts, axis=1)
    second_layer_terms = tuple(first + second for first, second in zip(*term_parts))
    hidden_gradient = (local_two + arrived_back.astype(jnp.float32)).astype(jnp.bfloat16)
    local_one, forward_rows_first, first_layer_terms = backward_layer(
        signal,
        first_history_rows,
        first_layer_stash,
        hidden_gradient,
        first_history_weight,
        first_current_weight,
        first_residual_weight,
    )
    leading_rows = forward_rows_first[:, :FIRST_DILATION, :]
    received_head_rows = shifted(leading_rows, "tm", -1)
    trailing_later_rows = jnp.concatenate(
        [forward_rows_first[:, FIRST_DILATION:, :], received_head_rows], axis=1
    )
    grad_signal = (local_one + trailing_later_rows.astype(jnp.float32)).astype(jnp.bfloat16)
    reduced = reduce_grads(tuple(first_layer_terms) + tuple(second_layer_terms), scale_factor)
    reduced_one, reduced_two = reduced[:3], reduced[3:]
    return (
        grad_signal,
        reduced_one[0],
        reduced_one[1],
        reduced_one[2],
        reduced_two[0],
        reduced_two[1],
        reduced_two[2],
    )


def solution(mesh):
    in_specs = (P("dp", "tm", None), P("dp", "tm", None), P(), P(), P(), P(), P(), P())
    out_specs = (P("dp", "tm", None), P(), P(), P(), P(), P(), P())
    return jax.shard_map(body, mesh=mesh, in_specs=in_specs, out_specs=out_specs, check_vma=False)
```

```python
import math

import jax
import jax.numpy as jnp
from jax import lax
from jax.sharding import PartitionSpec as P

FIRST_DILATION = 512
SECOND_DILATION = 8192


def shifted(value, axis, steps):
    count = lax.axis_size(axis)
    leading, last = (max(0, -steps), min(count, count - steps))
    return lax.ppermute(value, axis, [(source, source + steps) for source in range(leading, last)])


def forward_layer(input_traces, past_rows, tap_past, tap_now, mixing):
    channels = input_traces.shape[-1]
    flat_now = input_traces.reshape(-1, channels)
    flat_past = past_rows.reshape(-1, channels)
    pre_act = jnp.dot(flat_past, tap_past, preferred_element_type=jnp.float32) + jnp.dot(
        flat_now, tap_now, preferred_element_type=jnp.float32
    )
    half_width = pre_act.shape[1] // 2
    filter_part = jnp.tanh(pre_act[:, :half_width])
    gate_part = jax.nn.sigmoid(pre_act[:, half_width:])
    hidden = (filter_part * gate_part).astype(jnp.bfloat16)
    output = (
        flat_now.astype(jnp.float32) + jnp.dot(hidden, mixing, preferred_element_type=jnp.float32)
    ).astype(jnp.bfloat16)
    return (filter_part, gate_part, hidden, output.reshape(input_traces.shape))


def backward_layer(input_traces, past_rows, saved, incoming_gradient, tap_past, tap_now, mixing):
    filter_part, gate_part, hidden, output = saved
    channels = input_traces.shape[-1]
    flat_now = input_traces.reshape(-1, channels)
    flat_past = past_rows.reshape(-1, channels)
    flat_up = incoming_gradient.reshape(-1, channels)
    hidden_grad = jnp.dot(flat_up, mixing.T, preferred_element_type=jnp.float32)
    filter_grad = hidden_grad * gate_part * (1.0 - filter_part * filter_part)
    gate_grad = hidden_grad * filter_part * gate_part * (1.0 - gate_part)
    pre_grad = jnp.concatenate([filter_grad, gate_grad], axis=1).astype(jnp.bfloat16)
    past_term = jnp.einsum("rc,rg->cg", flat_past, pre_grad, preferred_element_type=jnp.float32)
    now_term = jnp.einsum("rc,rg->cg", flat_now, pre_grad, preferred_element_type=jnp.float32)
    mix_term = jnp.einsum("rh,rc->hc", hidden, flat_up, preferred_element_type=jnp.float32)
    ahead_rows = (
        jnp.dot(pre_grad, tap_past.T, preferred_element_type=jnp.float32)
        .astype(jnp.bfloat16)
        .reshape(input_traces.shape)
    )
    local_grad = (
        flat_up.astype(jnp.float32)
        + jnp.dot(pre_grad, tap_now.T, preferred_element_type=jnp.float32)
    ).reshape(input_traces.shape)
    return (local_grad, ahead_rows, (past_term, now_term, mix_term))


EARLY_STEPS = (("tm", 1), ("tm", 32))
HALVING_STEPS = (("dp", 1), ("tm", 2), ("dp", 4), ("dp", 2))
BUTTERFLY_STEPS = (("tm", 4), ("tm", 8), ("tm", 16))


def exchange(value, axis, mask):
    count = lax.axis_size(axis)
    return lax.ppermute(value, axis, [(source, source ^ mask) for source in range(count)])


def halve(flat, steps):
    for axis, mask in steps:
        half = flat.shape[0] // 2
        upper = (lax.axis_index(axis) & mask) != 0
        first, second = flat[:half], flat[half:]
        kept = jnp.where(upper, second, first)
        sent = jnp.where(upper, first, second)
        flat = kept + exchange(sent, axis, mask)
    return flat


def double(flat, steps):
    for axis, mask in reversed(steps):
        upper = (lax.axis_index(axis) & mask) != 0
        other = exchange(flat, axis, mask)
        flat = jnp.where(upper, jnp.concatenate([other, flat]), jnp.concatenate([flat, other]))
    return flat


def pack(term_list):
    width = term_list[0].shape[1]
    return jnp.concatenate([member.reshape(-1, width) for member in term_list])


def reduce_packed(early_pieces, shapes, scale_factor):
    joined = halve(jnp.concatenate(early_pieces), HALVING_STEPS)
    for axis, mask in BUTTERFLY_STEPS:
        joined = joined + exchange(joined, axis, mask)
    joined = (joined * scale_factor).astype(jnp.bfloat16)
    joined = double(joined, EARLY_STEPS + HALVING_STEPS)
    layers, early = len(early_pieces), 1 << len(EARLY_STEPS)
    block = joined.shape[0] // (layers * early)
    outputs = []
    for layer, layer_shapes in enumerate(shapes):
        rows = jnp.concatenate([joined[(index * layers + layer) * block:(index * layers + layer + 1) * block] for index in range(early)])
        start = 0
        for shape in layer_shapes:
            count = shape[0] * shape[1] // rows.shape[1]
            outputs.append(rows[start:start + count].reshape(shape))
            start += count
    return tuple(outputs)


def body(
    signal,
    cotangent,
    first_history_weight,
    first_current_weight,
    first_residual_weight,
    second_history_weight,
    second_current_weight,
    second_residual_weight,
):
    seq_count, number_of_steps, channels = signal.shape
    rows_all = seq_count * lax.axis_size("dp") * number_of_steps * lax.axis_size("tm")
    scale_factor = 1.0 / math.sqrt(rows_all)
    final_rows = signal[:, number_of_steps - FIRST_DILATION :, :]
    received_rows = shifted(final_rows, "tm", 1)
    first_history_rows = jnp.concatenate(
        [received_rows, signal[:, : number_of_steps - FIRST_DILATION, :]], axis=1
    )
    first_layer_stash = forward_layer(
        signal,
        first_history_rows,
        first_history_weight,
        first_current_weight,
        first_residual_weight,
    )
    hidden_activation = first_layer_stash[3]
    distant_offsets = SECOND_DILATION // number_of_steps
    chunk_rows = number_of_steps // 2
    local_parts, arrived_parts, term_parts, past_parts = [], [], [], []
    for chunk in range(2):
        rows = slice(chunk * chunk_rows, (chunk + 1) * chunk_rows)
        hidden_chunk = hidden_activation[:, rows, :]
        if chunk:
            hidden_chunk, _ = lax.optimization_barrier((hidden_chunk, past_parts[-1]))
        past_chunk = shifted(hidden_chunk, "tm", distant_offsets)
        if chunk:
            past_chunk, arrived_parts[-1] = lax.optimization_barrier((past_chunk, arrived_parts[-1]))
        past_parts.append(past_chunk)
        chunk_stash = forward_layer(
            hidden_chunk,
            past_chunk,
            second_history_weight,
            second_current_weight,
            second_residual_weight,
        )
        local_chunk, ahead_chunk, chunk_terms = backward_layer(
            hidden_chunk,
            past_chunk,
            chunk_stash,
            cotangent[:, rows, :],
            second_history_weight,
            second_current_weight,
            second_residual_weight,
        )
        local_parts.append(local_chunk)
        arrived_parts.append(shifted(ahead_chunk, "tm", -distant_offsets))
        term_parts.append(chunk_terms)
    local_two = jnp.concatenate(local_parts, axis=1)
    arrived_back = jnp.concatenate(arrived_parts, axis=1)
    second_layer_terms = tuple(first + second for first, second in zip(*term_parts))
    hidden_gradient = (local_two + arrived_back.astype(jnp.float32)).astype(jnp.bfloat16)
    early_two = halve(pack(second_layer_terms), EARLY_STEPS)
    hidden_gradient, early_two = lax.optimization_barrier((hidden_gradient, early_two))
    local_one, forward_rows_first, first_layer_terms = backward_layer(
        signal,
        first_history_rows,
        first_layer_stash,
        hidden_gradient,
        first_history_weight,
        first_current_weight,
        first_residual_weight,
    )
    leading_rows = forward_rows_first[:, :FIRST_DILATION, :]
    received_head_rows = shifted(leading_rows, "tm", -1)
    trailing_later_rows = jnp.concatenate(
        [forward_rows_first[:, FIRST_DILATION:, :], received_head_rows], axis=1
    )
    grad_signal = (local_one + trailing_later_rows.astype(jnp.float32)).astype(jnp.bfloat16)
    early_one = halve(pack(first_layer_terms), EARLY_STEPS)
    shapes = ([member.shape for member in first_layer_terms], [member.shape for member in second_layer_terms])
    reduced = reduce_packed([early_one, early_two], shapes, scale_factor)
    reduced_one, reduced_two = reduced[:3], reduced[3:]
    return (
        grad_signal,
        reduced_one[0],
        reduced_one[1],
        reduced_one[2],
        reduced_two[0],
        reduced_two[1],
        reduced_two[2],
    )


def solution(mesh):
    in_specs = (P("dp", "tm", None), P("dp", "tm", None), P(), P(), P(), P(), P(), P())
    out_specs = (P("dp", "tm", None), P(), P(), P(), P(), P(), P())
    return jax.shard_map(body, mesh=mesh, in_specs=in_specs, out_specs=out_specs, check_vma=False)
```

```python
import math

import jax
import jax.numpy as jnp
from jax import lax
from jax.sharding import PartitionSpec as P

FIRST_DILATION = 512
SECOND_DILATION = 8192


def shifted(value, axis, steps):
    count = lax.axis_size(axis)
    leading, last = (max(0, -steps), min(count, count - steps))
    return lax.ppermute(value, axis, [(source, source + steps) for source in range(leading, last)])


def forward_layer(input_traces, past_rows, tap_past, tap_now, mixing):
    channels = input_traces.shape[-1]
    flat_now = input_traces.reshape(-1, channels)
    flat_past = past_rows.reshape(-1, channels)
    pre_act = jnp.dot(flat_past, tap_past, preferred_element_type=jnp.float32) + jnp.dot(
        flat_now, tap_now, preferred_element_type=jnp.float32
    )
    half_width = pre_act.shape[1] // 2
    filter_part = jnp.tanh(pre_act[:, :half_width])
    gate_part = jax.nn.sigmoid(pre_act[:, half_width:])
    hidden = (filter_part * gate_part).astype(jnp.bfloat16)
    output = (
        flat_now.astype(jnp.float32) + jnp.dot(hidden, mixing, preferred_element_type=jnp.float32)
    ).astype(jnp.bfloat16)
    return (filter_part, gate_part, hidden, output.reshape(input_traces.shape))


def backward_layer(input_traces, past_rows, saved, incoming_gradient, tap_past, tap_now, mixing):
    filter_part, gate_part, hidden, output = saved
    channels = input_traces.shape[-1]
    flat_now = input_traces.reshape(-1, channels)
    flat_past = past_rows.reshape(-1, channels)
    flat_up = incoming_gradient.reshape(-1, channels)
    hidden_grad = jnp.dot(flat_up, mixing.T, preferred_element_type=jnp.float32)
    filter_grad = hidden_grad * gate_part * (1.0 - filter_part * filter_part)
    gate_grad = hidden_grad * filter_part * gate_part * (1.0 - gate_part)
    pre_grad = jnp.concatenate([filter_grad, gate_grad], axis=1).astype(jnp.bfloat16)
    past_term = jnp.einsum("rc,rg->cg", flat_past, pre_grad, preferred_element_type=jnp.float32)
    now_term = jnp.einsum("rc,rg->cg", flat_now, pre_grad, preferred_element_type=jnp.float32)
    mix_term = jnp.einsum("rh,rc->hc", hidden, flat_up, preferred_element_type=jnp.float32)
    ahead_rows = (
        jnp.dot(pre_grad, tap_past.T, preferred_element_type=jnp.float32)
        .astype(jnp.bfloat16)
        .reshape(input_traces.shape)
    )
    local_grad = (
        flat_up.astype(jnp.float32)
        + jnp.dot(pre_grad, tap_now.T, preferred_element_type=jnp.float32)
    ).reshape(input_traces.shape)
    return (local_grad, ahead_rows, (past_term, now_term, mix_term))


HALVING_STEPS = (("tm", 1), ("tm", 32), ("dp", 1), ("tm", 2), ("dp", 4), ("dp", 2))
PACKED_WIDTH = 512
BUTTERFLY_STEPS = (("tm", 4), ("tm", 8), ("tm", 16))


def exchange(value, axis, mask):
    count = lax.axis_size(axis)
    return lax.ppermute(value, axis, [(source, source ^ mask) for source in range(count)])


def reduce_grads(term_list, scale_factor):
    shapes = [member.shape for member in term_list]
    flat = jnp.concatenate([member.reshape(-1, PACKED_WIDTH) for member in term_list])
    for axis, mask in HALVING_STEPS:
        half = flat.shape[0] // 2
        upper = (lax.axis_index(axis) & mask) != 0
        first, second = flat[:half], flat[half:]
        kept = jnp.where(upper, second, first)
        sent = jnp.where(upper, first, second)
        flat = kept + exchange(sent, axis, mask)
    for axis, mask in BUTTERFLY_STEPS:
        flat = flat + exchange(flat, axis, mask)
    flat = (flat * scale_factor).astype(jnp.bfloat16)
    for axis, mask in reversed(HALVING_STEPS):
        upper = (lax.axis_index(axis) & mask) != 0
        other = exchange(flat, axis, mask)
        flat = jnp.where(upper, jnp.concatenate([other, flat]), jnp.concatenate([flat, other]))
    out, start = [], 0
    for shape in shapes:
        rows = shape[0] * shape[1] // PACKED_WIDTH
        out.append(flat[start:start + rows].reshape(shape))
        start += rows
    return tuple(out)


def body(
    signal,
    cotangent,
    first_history_weight,
    first_current_weight,
    first_residual_weight,
    second_history_weight,
    second_current_weight,
    second_residual_weight,
):
    seq_count, number_of_steps, channels = signal.shape
    rows_all = seq_count * lax.axis_size("dp") * number_of_steps * lax.axis_size("tm")
    scale_factor = 1.0 / math.sqrt(rows_all)
    final_rows = signal[:, number_of_steps - FIRST_DILATION :, :]
    received_rows = shifted(final_rows, "tm", 1)
    first_history_rows = jnp.concatenate(
        [received_rows, signal[:, : number_of_steps - FIRST_DILATION, :]], axis=1
    )
    first_layer_stash = forward_layer(
        signal,
        first_history_rows,
        first_history_weight,
        first_current_weight,
        first_residual_weight,
    )
    hidden_activation = first_layer_stash[3]
    distant_offsets = SECOND_DILATION // number_of_steps
    chunk_rows = number_of_steps // 2
    local_parts, arrived_parts, term_parts, past_parts = [], [], [], []
    for chunk in range(2):
        rows = slice(chunk * chunk_rows, (chunk + 1) * chunk_rows)
        hidden_chunk = hidden_activation[:, rows, :]
        if chunk:
            hidden_chunk, _ = lax.optimization_barrier((hidden_chunk, past_parts[-1]))
        past_chunk = shifted(hidden_chunk, "tm", distant_offsets)
        past_parts.append(past_chunk)
        chunk_stash = forward_layer(
            hidden_chunk,
            past_chunk,
            second_history_weight,
            second_current_weight,
            second_residual_weight,
        )
        local_chunk, ahead_chunk, chunk_terms = backward_layer(
            hidden_chunk,
            past_chunk,
            chunk_stash,
            cotangent[:, rows, :],
            second_history_weight,
            second_current_weight,
            second_residual_weight,
        )
        local_parts.append(local_chunk)
        arrived_parts.append(shifted(ahead_chunk, "tm", -distant_offsets))
        term_parts.append(chunk_terms)
    local_two = jnp.concatenate(local_parts, axis=1)
    arrived_back = jnp.concatenate(arrived_parts, axis=1)
    second_layer_terms = tuple(first + second for first, second in zip(*term_parts))
    hidden_gradient = (local_two + arrived_back.astype(jnp.float32)).astype(jnp.bfloat16)
    local_one, forward_rows_first, first_layer_terms = backward_layer(
        signal,
        first_history_rows,
        first_layer_stash,
        hidden_gradient,
        first_history_weight,
        first_current_weight,
        first_residual_weight,
    )
    leading_rows = forward_rows_first[:, :FIRST_DILATION, :]
    received_head_rows = shifted(leading_rows, "tm", -1)
    trailing_later_rows = jnp.concatenate(
        [forward_rows_first[:, FIRST_DILATION:, :], received_head_rows], axis=1
    )
    grad_signal = (local_one + trailing_later_rows.astype(jnp.float32)).astype(jnp.bfloat16)
    reduced = reduce_grads(tuple(first_layer_terms) + tuple(second_layer_terms), scale_factor)
    reduced_one, reduced_two = reduced[:3], reduced[3:]
    return (
        grad_signal,
        reduced_one[0],
        reduced_one[1],
        reduced_one[2],
        reduced_two[0],
        reduced_two[1],
        reduced_two[2],
    )


def solution(mesh):
    in_specs = (P("dp", "tm", None), P("dp", "tm", None), P(), P(), P(), P(), P(), P())
    out_specs = (P("dp", "tm", None), P(), P(), P(), P(), P(), P())
    return jax.shard_map(body, mesh=mesh, in_specs=in_specs, out_specs=out_specs, check_vma=False)
```

```python
import math

import jax
import jax.numpy as jnp
from jax import lax
from jax.sharding import PartitionSpec as P

FIRST_DILATION = 512
SECOND_DILATION = 8192


def shifted(value, axis, steps):
    count = lax.axis_size(axis)
    leading, last = (max(0, -steps), min(count, count - steps))
    return lax.ppermute(value, axis, [(source, source + steps) for source in range(leading, last)])


def forward_layer(input_traces, past_rows, tap_past, tap_now, mixing):
    channels = input_traces.shape[-1]
    flat_now = input_traces.reshape(-1, channels)
    flat_past = past_rows.reshape(-1, channels)
    pre_act = jnp.dot(flat_past, tap_past, preferred_element_type=jnp.float32) + jnp.dot(
        flat_now, tap_now, preferred_element_type=jnp.float32
    )
    half_width = pre_act.shape[1] // 2
    filter_part = jnp.tanh(pre_act[:, :half_width])
    gate_part = jax.nn.sigmoid(pre_act[:, half_width:])
    hidden = (filter_part * gate_part).astype(jnp.bfloat16)
    output = (
        flat_now.astype(jnp.float32) + jnp.dot(hidden, mixing, preferred_element_type=jnp.float32)
    ).astype(jnp.bfloat16)
    return (filter_part, gate_part, hidden, output.reshape(input_traces.shape))


def backward_layer(input_traces, past_rows, saved, incoming_gradient, tap_past, tap_now, mixing):
    filter_part, gate_part, hidden, output = saved
    channels = input_traces.shape[-1]
    flat_now = input_traces.reshape(-1, channels)
    flat_past = past_rows.reshape(-1, channels)
    flat_up = incoming_gradient.reshape(-1, channels)
    hidden_grad = jnp.dot(flat_up, mixing.T, preferred_element_type=jnp.float32)
    filter_grad = hidden_grad * gate_part * (1.0 - filter_part * filter_part)
    gate_grad = hidden_grad * filter_part * gate_part * (1.0 - gate_part)
    pre_grad = jnp.concatenate([filter_grad, gate_grad], axis=1).astype(jnp.bfloat16)
    past_term = jnp.einsum("rc,rg->cg", flat_past, pre_grad, preferred_element_type=jnp.float32)
    now_term = jnp.einsum("rc,rg->cg", flat_now, pre_grad, preferred_element_type=jnp.float32)
    mix_term = jnp.einsum("rh,rc->hc", hidden, flat_up, preferred_element_type=jnp.float32)
    ahead_rows = (
        jnp.dot(pre_grad, tap_past.T, preferred_element_type=jnp.float32)
        .astype(jnp.bfloat16)
        .reshape(input_traces.shape)
    )
    local_grad = (
        flat_up.astype(jnp.float32)
        + jnp.dot(pre_grad, tap_now.T, preferred_element_type=jnp.float32)
    ).reshape(input_traces.shape)
    return (local_grad, ahead_rows, (past_term, now_term, mix_term))


HALVING_STEPS = (("tm", 1), ("tm", 32), ("dp", 1), ("tm", 2), ("dp", 4), ("dp", 2))
PACKED_WIDTH = 512
BUTTERFLY_STEPS = (("tm", 4), ("tm", 8), ("tm", 16))


def exchange(value, axis, mask):
    count = lax.axis_size(axis)
    return lax.ppermute(value, axis, [(source, source ^ mask) for source in range(count)])


def reduce_grads(term_list, scale_factor, companion):
    shapes = [member.shape for member in term_list]
    flat = jnp.concatenate([member.reshape(-1, PACKED_WIDTH) for member in term_list])
    for axis, mask in HALVING_STEPS:
        half = flat.shape[0] // 2
        upper = (lax.axis_index(axis) & mask) != 0
        first, second = flat[:half], flat[half:]
        kept = jnp.where(upper, second, first)
        sent = jnp.where(upper, first, second)
        flat = kept + exchange(sent, axis, mask)
        if mask == 32:
            flat, companion = lax.optimization_barrier((flat, companion))
    for axis, mask in BUTTERFLY_STEPS:
        flat = flat + exchange(flat, axis, mask)
    flat = (flat * scale_factor).astype(jnp.bfloat16)
    for axis, mask in reversed(HALVING_STEPS):
        upper = (lax.axis_index(axis) & mask) != 0
        other = exchange(flat, axis, mask)
        flat = jnp.where(upper, jnp.concatenate([other, flat]), jnp.concatenate([flat, other]))
    out, start = [], 0
    for shape in shapes:
        rows = shape[0] * shape[1] // PACKED_WIDTH
        out.append(flat[start:start + rows].reshape(shape))
        start += rows
    return tuple(out), companion


def body(
    signal,
    cotangent,
    first_history_weight,
    first_current_weight,
    first_residual_weight,
    second_history_weight,
    second_current_weight,
    second_residual_weight,
):
    seq_count, number_of_steps, channels = signal.shape
    rows_all = seq_count * lax.axis_size("dp") * number_of_steps * lax.axis_size("tm")
    scale_factor = 1.0 / math.sqrt(rows_all)
    final_rows = signal[:, number_of_steps - FIRST_DILATION :, :]
    received_rows = shifted(final_rows, "tm", 1)
    first_history_rows = jnp.concatenate(
        [received_rows, signal[:, : number_of_steps - FIRST_DILATION, :]], axis=1
    )
    first_layer_stash = forward_layer(
        signal,
        first_history_rows,
        first_history_weight,
        first_current_weight,
        first_residual_weight,
    )
    hidden_activation = first_layer_stash[3]
    distant_offsets = SECOND_DILATION // number_of_steps
    chunk_rows = number_of_steps // 2
    local_parts, arrived_parts, term_parts, past_parts = [], [], [], []
    for chunk in range(2):
        rows = slice(chunk * chunk_rows, (chunk + 1) * chunk_rows)
        hidden_chunk = hidden_activation[:, rows, :]
        if chunk:
            hidden_chunk, _ = lax.optimization_barrier((hidden_chunk, past_parts[-1]))
        past_chunk = shifted(hidden_chunk, "tm", distant_offsets)
        past_parts.append(past_chunk)
        chunk_stash = forward_layer(
            hidden_chunk,
            past_chunk,
            second_history_weight,
            second_current_weight,
            second_residual_weight,
        )
        local_chunk, ahead_chunk, chunk_terms = backward_layer(
            hidden_chunk,
            past_chunk,
            chunk_stash,
            cotangent[:, rows, :],
            second_history_weight,
            second_current_weight,
            second_residual_weight,
        )
        local_parts.append(local_chunk)
        arrived_parts.append(shifted(ahead_chunk, "tm", -distant_offsets))
        term_parts.append(chunk_terms)
    local_two = jnp.concatenate(local_parts, axis=1)
    arrived_back = jnp.concatenate(arrived_parts, axis=1)
    second_layer_terms = tuple(first + second for first, second in zip(*term_parts))
    hidden_gradient = (local_two + arrived_back.astype(jnp.float32)).astype(jnp.bfloat16)
    local_one, forward_rows_first, first_layer_terms = backward_layer(
        signal,
        first_history_rows,
        first_layer_stash,
        hidden_gradient,
        first_history_weight,
        first_current_weight,
        first_residual_weight,
    )
    leading_rows = forward_rows_first[:, :FIRST_DILATION, :]
    received_head_rows = shifted(leading_rows, "tm", -1)
    trailing_later_rows = jnp.concatenate(
        [forward_rows_first[:, FIRST_DILATION:, :], received_head_rows], axis=1
    )
    grad_signal = (local_one + trailing_later_rows.astype(jnp.float32)).astype(jnp.bfloat16)
    reduced, grad_signal = reduce_grads(tuple(first_layer_terms) + tuple(second_layer_terms), scale_factor, grad_signal)
    reduced_one, reduced_two = reduced[:3], reduced[3:]
    return (
        grad_signal,
        reduced_one[0],
        reduced_one[1],
        reduced_one[2],
        reduced_two[0],
        reduced_two[1],
        reduced_two[2],
    )


def solution(mesh):
    in_specs = (P("dp", "tm", None), P("dp", "tm", None), P(), P(), P(), P(), P(), P())
    out_specs = (P("dp", "tm", None), P(), P(), P(), P(), P(), P())
    return jax.shard_map(body, mesh=mesh, in_specs=in_specs, out_specs=out_specs, check_vma=False)
```

```python
import math

import jax
import jax.numpy as jnp
from jax import lax
from jax.sharding import PartitionSpec as P

FIRST_DILATION = 512
SECOND_DILATION = 8192


def shifted(value, axis, steps):
    count = lax.axis_size(axis)
    leading, last = (max(0, -steps), min(count, count - steps))
    return lax.ppermute(value, axis, [(source, source + steps) for source in range(leading, last)])


def forward_layer(input_traces, past_rows, tap_past, tap_now, mixing):
    channels = input_traces.shape[-1]
    flat_now = input_traces.reshape(-1, channels)
    flat_past = past_rows.reshape(-1, channels)
    pre_act = jnp.dot(flat_past, tap_past, preferred_element_type=jnp.float32) + jnp.dot(
        flat_now, tap_now, preferred_element_type=jnp.float32
    )
    half_width = pre_act.shape[1] // 2
    filter_part = jnp.tanh(pre_act[:, :half_width])
    gate_part = jax.nn.sigmoid(pre_act[:, half_width:])
    hidden = (filter_part * gate_part).astype(jnp.bfloat16)
    output = (
        flat_now.astype(jnp.float32) + jnp.dot(hidden, mixing, preferred_element_type=jnp.float32)
    ).astype(jnp.bfloat16)
    return (filter_part, gate_part, hidden, output.reshape(input_traces.shape))


def backward_layer(input_traces, past_rows, saved, incoming_gradient, tap_past, tap_now, mixing):
    filter_part, gate_part, hidden, output = saved
    channels = input_traces.shape[-1]
    flat_now = input_traces.reshape(-1, channels)
    flat_past = past_rows.reshape(-1, channels)
    flat_up = incoming_gradient.reshape(-1, channels)
    hidden_grad = jnp.dot(flat_up, mixing.T, preferred_element_type=jnp.float32)
    filter_grad = hidden_grad * gate_part * (1.0 - filter_part * filter_part)
    gate_grad = hidden_grad * filter_part * gate_part * (1.0 - gate_part)
    pre_grad = jnp.concatenate([filter_grad, gate_grad], axis=1).astype(jnp.bfloat16)
    past_term = jnp.einsum("rc,rg->cg", flat_past, pre_grad, preferred_element_type=jnp.float32)
    now_term = jnp.einsum("rc,rg->cg", flat_now, pre_grad, preferred_element_type=jnp.float32)
    mix_term = jnp.einsum("rh,rc->hc", hidden, flat_up, preferred_element_type=jnp.float32)
    ahead_rows = (
        jnp.dot(pre_grad, tap_past.T, preferred_element_type=jnp.float32)
        .astype(jnp.bfloat16)
        .reshape(input_traces.shape)
    )
    local_grad = (
        flat_up.astype(jnp.float32)
        + jnp.dot(pre_grad, tap_now.T, preferred_element_type=jnp.float32)
    ).reshape(input_traces.shape)
    return (local_grad, ahead_rows, (past_term, now_term, mix_term))


HALVING_STEPS = (("tm", 1), ("tm", 32), ("dp", 1), ("tm", 2), ("dp", 4), ("dp", 2))
BUTTERFLY_STEPS = (("tm", 4), ("tm", 8), ("tm", 16))


def exchange(value, axis, mask):
    count = lax.axis_size(axis)
    return lax.ppermute(value, axis, [(source, source ^ mask) for source in range(count)])


def reduce_grads(term_list, scale_factor, companion):
    past_one, now_one, mix_one, past_two, now_two, mix_two = term_list
    blocks = (past_one, now_one, past_two, now_two, jnp.concatenate([mix_one, mix_two], axis=1))
    flat = jnp.concatenate(blocks)
    for axis, mask in HALVING_STEPS:
        half = flat.shape[0] // 2
        upper = (lax.axis_index(axis) & mask) != 0
        first, second = flat[:half], flat[half:]
        kept = jnp.where(upper, second, first)
        sent = jnp.where(upper, first, second)
        flat = kept + exchange(sent, axis, mask)
        if mask == 32:
            flat, companion = lax.optimization_barrier((flat, companion))
    for axis, mask in BUTTERFLY_STEPS:
        flat = flat + exchange(flat, axis, mask)
    flat = (flat * scale_factor).astype(jnp.bfloat16)
    for axis, mask in reversed(HALVING_STEPS):
        upper = (lax.axis_index(axis) & mask) != 0
        other = exchange(flat, axis, mask)
        flat = jnp.where(upper, jnp.concatenate([other, flat]), jnp.concatenate([flat, other]))
    rows = past_one.shape[0]
    parts = [flat[index * rows:(index + 1) * rows] for index in range(len(blocks))]
    mix_width = mix_one.shape[1]
    out = (parts[0], parts[1], parts[4][:, :mix_width], parts[2], parts[3], parts[4][:, mix_width:])
    return out, companion


def body(
    signal,
    cotangent,
    first_history_weight,
    first_current_weight,
    first_residual_weight,
    second_history_weight,
    second_current_weight,
    second_residual_weight,
):
    seq_count, number_of_steps, channels = signal.shape
    rows_all = seq_count * lax.axis_size("dp") * number_of_steps * lax.axis_size("tm")
    scale_factor = 1.0 / math.sqrt(rows_all)
    final_rows = signal[:, number_of_steps - FIRST_DILATION :, :]
    received_rows = shifted(final_rows, "tm", 1)
    first_history_rows = jnp.concatenate(
        [received_rows, signal[:, : number_of_steps - FIRST_DILATION, :]], axis=1
    )
    first_layer_stash = forward_layer(
        signal,
        first_history_rows,
        first_history_weight,
        first_current_weight,
        first_residual_weight,
    )
    hidden_activation = first_layer_stash[3]
    distant_offsets = SECOND_DILATION // number_of_steps
    chunk_rows = number_of_steps // 2
    local_parts, arrived_parts, term_parts, past_parts = [], [], [], []
    for chunk in range(2):
        rows = slice(chunk * chunk_rows, (chunk + 1) * chunk_rows)
        hidden_chunk = hidden_activation[:, rows, :]
        if chunk:
            hidden_chunk, _ = lax.optimization_barrier((hidden_chunk, past_parts[-1]))
        past_chunk = shifted(hidden_chunk, "tm", distant_offsets)
        past_parts.append(past_chunk)
        chunk_stash = forward_layer(
            hidden_chunk,
            past_chunk,
            second_history_weight,
            second_current_weight,
            second_residual_weight,
        )
        local_chunk, ahead_chunk, chunk_terms = backward_layer(
            hidden_chunk,
            past_chunk,
            chunk_stash,
            cotangent[:, rows, :],
            second_history_weight,
            second_current_weight,
            second_residual_weight,
        )
        local_parts.append(local_chunk)
        arrived_parts.append(shifted(ahead_chunk, "tm", -distant_offsets))
        term_parts.append(chunk_terms)
    local_two = jnp.concatenate(local_parts, axis=1)
    arrived_back = jnp.concatenate(arrived_parts, axis=1)
    second_layer_terms = tuple(first + second for first, second in zip(*term_parts))
    hidden_gradient = (local_two + arrived_back.astype(jnp.float32)).astype(jnp.bfloat16)
    local_one, forward_rows_first, first_layer_terms = backward_layer(
        signal,
        first_history_rows,
        first_layer_stash,
        hidden_gradient,
        first_history_weight,
        first_current_weight,
        first_residual_weight,
    )
    leading_rows = forward_rows_first[:, :FIRST_DILATION, :]
    received_head_rows = shifted(leading_rows, "tm", -1)
    trailing_later_rows = jnp.concatenate(
        [forward_rows_first[:, FIRST_DILATION:, :], received_head_rows], axis=1
    )
    grad_signal = (local_one + trailing_later_rows.astype(jnp.float32)).astype(jnp.bfloat16)
    reduced, grad_signal = reduce_grads(tuple(first_layer_terms) + tuple(second_layer_terms), scale_factor, grad_signal)
    reduced_one, reduced_two = reduced[:3], reduced[3:]
    return (
        grad_signal,
        reduced_one[0],
        reduced_one[1],
        reduced_one[2],
        reduced_two[0],
        reduced_two[1],
        reduced_two[2],
    )


def solution(mesh):
    in_specs = (P("dp", "tm", None), P("dp", "tm", None), P(), P(), P(), P(), P(), P())
    out_specs = (P("dp", "tm", None), P(), P(), P(), P(), P(), P())
    return jax.shard_map(body, mesh=mesh, in_specs=in_specs, out_specs=out_specs, check_vma=False)
```

```python
import math

import jax
import jax.numpy as jnp
from jax import lax
from jax.sharding import PartitionSpec as P

FIRST_DILATION = 512
SECOND_DILATION = 8192


def shifted(value, axis, steps):
    count = lax.axis_size(axis)
    leading, last = (max(0, -steps), min(count, count - steps))
    return lax.ppermute(value, axis, [(source, source + steps) for source in range(leading, last)])


def forward_layer(input_traces, past_rows, tap_past, tap_now, mixing):
    channels = input_traces.shape[-1]
    flat_now = input_traces.reshape(-1, channels)
    flat_past = past_rows.reshape(-1, channels)
    pre_act = jnp.dot(flat_past, tap_past, preferred_element_type=jnp.float32) + jnp.dot(
        flat_now, tap_now, preferred_element_type=jnp.float32
    )
    half_width = pre_act.shape[1] // 2
    filter_part = jnp.tanh(pre_act[:, :half_width])
    gate_part = jax.nn.sigmoid(pre_act[:, half_width:])
    hidden = (filter_part * gate_part).astype(jnp.bfloat16)
    output = (
        flat_now.astype(jnp.float32) + jnp.dot(hidden, mixing, preferred_element_type=jnp.float32)
    ).astype(jnp.bfloat16)
    return (filter_part, gate_part, hidden, output.reshape(input_traces.shape))


def backward_layer(input_traces, past_rows, saved, incoming_gradient, tap_past, tap_now, mixing):
    filter_part, gate_part, hidden, output = saved
    channels = input_traces.shape[-1]
    flat_now = input_traces.reshape(-1, channels)
    flat_past = past_rows.reshape(-1, channels)
    flat_up = incoming_gradient.reshape(-1, channels)
    hidden_grad = jnp.dot(flat_up, mixing.T, preferred_element_type=jnp.float32)
    filter_grad = hidden_grad * gate_part * (1.0 - filter_part * filter_part)
    gate_grad = hidden_grad * filter_part * gate_part * (1.0 - gate_part)
    pre_grad = jnp.concatenate([filter_grad, gate_grad], axis=1).astype(jnp.bfloat16)
    past_term = jnp.einsum("rc,rg->cg", flat_past, pre_grad, preferred_element_type=jnp.float32)
    now_term = jnp.einsum("rc,rg->cg", flat_now, pre_grad, preferred_element_type=jnp.float32)
    mix_term = jnp.einsum("rh,rc->hc", hidden, flat_up, preferred_element_type=jnp.float32)
    ahead_rows = (
        jnp.dot(pre_grad, tap_past.T, preferred_element_type=jnp.float32)
        .astype(jnp.bfloat16)
        .reshape(input_traces.shape)
    )
    local_grad = (
        flat_up.astype(jnp.float32)
        + jnp.dot(pre_grad, tap_now.T, preferred_element_type=jnp.float32)
    ).reshape(input_traces.shape)
    return (local_grad, ahead_rows, (past_term, now_term, mix_term))


HALVING_STEPS = ((1, 1), (32, 64), (64, 32), (2, 2), (256, 256), (128, 128))
AXES = ("dp", "tm")
BUTTERFLY_STEPS = (("tm", 4), ("tm", 8), ("tm", 16))


def paired(value, masks):
    count = lax.axis_size(AXES)
    pairs = [(source, source ^ masks[source & 1]) for source in range(count)]
    return lax.ppermute(value, AXES, pairs)


def upper_of(masks):
    index = lax.axis_index(AXES)
    return (index & jnp.where((index & 1) != 0, masks[1], masks[0])) != 0


def exchange(value, axis, mask):
    count = lax.axis_size(axis)
    return lax.ppermute(value, axis, [(source, source ^ mask) for source in range(count)])


def reduce_grads(term_list, scale_factor, companion):
    past_one, now_one, mix_one, past_two, now_two, mix_two = term_list
    blocks = (past_one, now_one, past_two, now_two, jnp.concatenate([mix_one, mix_two], axis=1))
    flat = jnp.concatenate(blocks)
    for step, masks in enumerate(HALVING_STEPS):
        half = flat.shape[0] // 2
        upper = upper_of(masks)
        first, second = flat[:half], flat[half:]
        kept = jnp.where(upper, second, first)
        sent = jnp.where(upper, first, second)
        flat = kept + paired(sent, masks)
        if step == 1:
            flat, companion = lax.optimization_barrier((flat, companion))
    for axis, mask in BUTTERFLY_STEPS:
        flat = flat + exchange(flat, axis, mask)
    flat = (flat * scale_factor).astype(jnp.bfloat16)
    for masks in reversed(HALVING_STEPS):
        upper = upper_of(masks)
        other = paired(flat, masks)
        flat = jnp.where(upper, jnp.concatenate([other, flat]), jnp.concatenate([flat, other]))
    rows = past_one.shape[0]
    parts = [flat[index * rows:(index + 1) * rows] for index in range(len(blocks))]
    mix_width = mix_one.shape[1]
    out = (parts[0], parts[1], parts[4][:, :mix_width], parts[2], parts[3], parts[4][:, mix_width:])
    return out, companion


def body(
    signal,
    cotangent,
    first_history_weight,
    first_current_weight,
    first_residual_weight,
    second_history_weight,
    second_current_weight,
    second_residual_weight,
):
    seq_count, number_of_steps, channels = signal.shape
    rows_all = seq_count * lax.axis_size("dp") * number_of_steps * lax.axis_size("tm")
    scale_factor = 1.0 / math.sqrt(rows_all)
    final_rows = signal[:, number_of_steps - FIRST_DILATION :, :]
    received_rows = shifted(final_rows, "tm", 1)
    first_history_rows = jnp.concatenate(
        [received_rows, signal[:, : number_of_steps - FIRST_DILATION, :]], axis=1
    )
    first_layer_stash = forward_layer(
        signal,
        first_history_rows,
        first_history_weight,
        first_current_weight,
        first_residual_weight,
    )
    hidden_activation = first_layer_stash[3]
    distant_offsets = SECOND_DILATION // number_of_steps
    chunk_rows = number_of_steps // 2
    local_parts, arrived_parts, term_parts, past_parts = [], [], [], []
    for chunk in range(2):
        rows = slice(chunk * chunk_rows, (chunk + 1) * chunk_rows)
        hidden_chunk = hidden_activation[:, rows, :]
        if chunk:
            hidden_chunk, _ = lax.optimization_barrier((hidden_chunk, past_parts[-1]))
        past_chunk = shifted(hidden_chunk, "tm", distant_offsets)
        past_parts.append(past_chunk)
        chunk_stash = forward_layer(
            hidden_chunk,
            past_chunk,
            second_history_weight,
            second_current_weight,
            second_residual_weight,
        )
        local_chunk, ahead_chunk, chunk_terms = backward_layer(
            hidden_chunk,
            past_chunk,
            chunk_stash,
            cotangent[:, rows, :],
            second_history_weight,
            second_current_weight,
            second_residual_weight,
        )
        local_parts.append(local_chunk)
        arrived_parts.append(shifted(ahead_chunk, "tm", -distant_offsets))
        term_parts.append(chunk_terms)
    local_two = jnp.concatenate(local_parts, axis=1)
    arrived_back = jnp.concatenate(arrived_parts, axis=1)
    second_layer_terms = tuple(first + second for first, second in zip(*term_parts))
    hidden_gradient = (local_two + arrived_back.astype(jnp.float32)).astype(jnp.bfloat16)
    local_one, forward_rows_first, first_layer_terms = backward_layer(
        signal,
        first_history_rows,
        first_layer_stash,
        hidden_gradient,
        first_history_weight,
        first_current_weight,
        first_residual_weight,
    )
    leading_rows = forward_rows_first[:, :FIRST_DILATION, :]
    received_head_rows = shifted(leading_rows, "tm", -1)
    trailing_later_rows = jnp.concatenate(
        [forward_rows_first[:, FIRST_DILATION:, :], received_head_rows], axis=1
    )
    grad_signal = (local_one + trailing_later_rows.astype(jnp.float32)).astype(jnp.bfloat16)
    reduced, grad_signal = reduce_grads(tuple(first_layer_terms) + tuple(second_layer_terms), scale_factor, grad_signal)
    reduced_one, reduced_two = reduced[:3], reduced[3:]
    return (
        grad_signal,
        reduced_one[0],
        reduced_one[1],
        reduced_one[2],
        reduced_two[0],
        reduced_two[1],
        reduced_two[2],
    )


def solution(mesh):
    in_specs = (P("dp", "tm", None), P("dp", "tm", None), P(), P(), P(), P(), P(), P())
    out_specs = (P("dp", "tm", None), P(), P(), P(), P(), P(), P())
    return jax.shard_map(body, mesh=mesh, in_specs=in_specs, out_specs=out_specs, check_vma=False)
```

```python
import math

import jax
import jax.numpy as jnp
from jax import lax
from jax.sharding import PartitionSpec as P

FIRST_DILATION = 512
SECOND_DILATION = 8192


def shifted(value, axis, steps):
    count = lax.axis_size(axis)
    leading, last = (max(0, -steps), min(count, count - steps))
    return lax.ppermute(value, axis, [(source, source + steps) for source in range(leading, last)])


def forward_layer(input_traces, past_rows, tap_past, tap_now, mixing):
    channels = input_traces.shape[-1]
    flat_now = input_traces.reshape(-1, channels)
    flat_past = past_rows.reshape(-1, channels)
    pre_act = jnp.dot(flat_past, tap_past, preferred_element_type=jnp.float32) + jnp.dot(
        flat_now, tap_now, preferred_element_type=jnp.float32
    )
    half_width = pre_act.shape[1] // 2
    filter_part = jnp.tanh(pre_act[:, :half_width])
    gate_part = jax.nn.sigmoid(pre_act[:, half_width:])
    hidden = (filter_part * gate_part).astype(jnp.bfloat16)
    output = (
        flat_now.astype(jnp.float32) + jnp.dot(hidden, mixing, preferred_element_type=jnp.float32)
    ).astype(jnp.bfloat16)
    return (filter_part, gate_part, hidden, output.reshape(input_traces.shape))


def backward_layer(input_traces, past_rows, saved, incoming_gradient, tap_past, tap_now, mixing):
    filter_part, gate_part, hidden, output = saved
    channels = input_traces.shape[-1]
    flat_now = input_traces.reshape(-1, channels)
    flat_past = past_rows.reshape(-1, channels)
    flat_up = incoming_gradient.reshape(-1, channels)
    hidden_grad = jnp.dot(flat_up, mixing.T, preferred_element_type=jnp.float32)
    filter_grad = hidden_grad * gate_part * (1.0 - filter_part * filter_part)
    gate_grad = hidden_grad * filter_part * gate_part * (1.0 - gate_part)
    pre_grad = jnp.concatenate([filter_grad, gate_grad], axis=1).astype(jnp.bfloat16)
    past_term = jnp.einsum("rc,rg->cg", flat_past, pre_grad, preferred_element_type=jnp.float32)
    now_term = jnp.einsum("rc,rg->cg", flat_now, pre_grad, preferred_element_type=jnp.float32)
    mix_term = jnp.einsum("rh,rc->hc", hidden, flat_up, preferred_element_type=jnp.float32)
    ahead_rows = (
        jnp.dot(pre_grad, tap_past.T, preferred_element_type=jnp.float32)
        .astype(jnp.bfloat16)
        .reshape(input_traces.shape)
    )
    local_grad = (
        flat_up.astype(jnp.float32)
        + jnp.dot(pre_grad, tap_now.T, preferred_element_type=jnp.float32)
    ).reshape(input_traces.shape)
    return (local_grad, ahead_rows, (past_term, now_term, mix_term))


HALVING_STEPS = ((1, 1), (32, 64), (64, 32), (2, 256), (256, 2), (128, 128))
AXES = ("dp", "tm")
BUTTERFLY_STEPS = (("tm", 4), ("tm", 8), ("tm", 16))


def paired(value, masks):
    count = lax.axis_size(AXES)
    pairs = [(source, source ^ masks[source & 1]) for source in range(count)]
    return lax.ppermute(value, AXES, pairs)


def upper_of(masks):
    index = lax.axis_index(AXES)
    return (index & jnp.where((index & 1) != 0, masks[1], masks[0])) != 0


def exchange(value, axis, mask):
    count = lax.axis_size(axis)
    return lax.ppermute(value, axis, [(source, source ^ mask) for source in range(count)])


def reduce_grads(term_list, scale_factor, companion):
    past_one, now_one, mix_one, past_two, now_two, mix_two = term_list
    blocks = (past_one, now_one, past_two, now_two, jnp.concatenate([mix_one, mix_two], axis=1))
    flat = jnp.concatenate(blocks)
    for step, masks in enumerate(HALVING_STEPS):
        half = flat.shape[0] // 2
        upper = upper_of(masks)
        first, second = flat[:half], flat[half:]
        kept = jnp.where(upper, second, first)
        sent = jnp.where(upper, first, second)
        flat = kept + paired(sent, masks)
        if step == 1:
            flat, companion = lax.optimization_barrier((flat, companion))
    for axis, mask in BUTTERFLY_STEPS:
        flat = flat + exchange(flat, axis, mask)
    flat = (flat * scale_factor).astype(jnp.bfloat16)
    for masks in reversed(HALVING_STEPS):
        upper = upper_of(masks)
        other = paired(flat, masks)
        flat = jnp.where(upper, jnp.concatenate([other, flat]), jnp.concatenate([flat, other]))
    rows = past_one.shape[0]
    parts = [flat[index * rows:(index + 1) * rows] for index in range(len(blocks))]
    mix_width = mix_one.shape[1]
    out = (parts[0], parts[1], parts[4][:, :mix_width], parts[2], parts[3], parts[4][:, mix_width:])
    return out, companion


def body(
    signal,
    cotangent,
    first_history_weight,
    first_current_weight,
    first_residual_weight,
    second_history_weight,
    second_current_weight,
    second_residual_weight,
):
    seq_count, number_of_steps, channels = signal.shape
    rows_all = seq_count * lax.axis_size("dp") * number_of_steps * lax.axis_size("tm")
    scale_factor = 1.0 / math.sqrt(rows_all)
    final_rows = signal[:, number_of_steps - FIRST_DILATION :, :]
    received_rows = shifted(final_rows, "tm", 1)
    first_history_rows = jnp.concatenate(
        [received_rows, signal[:, : number_of_steps - FIRST_DILATION, :]], axis=1
    )
    first_layer_stash = forward_layer(
        signal,
        first_history_rows,
        first_history_weight,
        first_current_weight,
        first_residual_weight,
    )
    hidden_activation = first_layer_stash[3]
    distant_offsets = SECOND_DILATION // number_of_steps
    chunk_rows = number_of_steps // 2
    local_parts, arrived_parts, term_parts, past_parts = [], [], [], []
    for chunk in range(2):
        rows = slice(chunk * chunk_rows, (chunk + 1) * chunk_rows)
        hidden_chunk = hidden_activation[:, rows, :]
        if chunk:
            hidden_chunk, _ = lax.optimization_barrier((hidden_chunk, past_parts[-1]))
        past_chunk = shifted(hidden_chunk, "tm", distant_offsets)
        past_parts.append(past_chunk)
        chunk_stash = forward_layer(
            hidden_chunk,
            past_chunk,
            second_history_weight,
            second_current_weight,
            second_residual_weight,
        )
        local_chunk, ahead_chunk, chunk_terms = backward_layer(
            hidden_chunk,
            past_chunk,
            chunk_stash,
            cotangent[:, rows, :],
            second_history_weight,
            second_current_weight,
            second_residual_weight,
        )
        local_parts.append(local_chunk)
        arrived_parts.append(shifted(ahead_chunk, "tm", -distant_offsets))
        term_parts.append(chunk_terms)
    local_two = jnp.concatenate(local_parts, axis=1)
    arrived_back = jnp.concatenate(arrived_parts, axis=1)
    second_layer_terms = tuple(first + second for first, second in zip(*term_parts))
    hidden_gradient = (local_two + arrived_back.astype(jnp.float32)).astype(jnp.bfloat16)
    local_one, forward_rows_first, first_layer_terms = backward_layer(
        signal,
        first_history_rows,
        first_layer_stash,
        hidden_gradient,
        first_history_weight,
        first_current_weight,
        first_residual_weight,
    )
    leading_rows = forward_rows_first[:, :FIRST_DILATION, :]
    received_head_rows = shifted(leading_rows, "tm", -1)
    trailing_later_rows = jnp.concatenate(
        [forward_rows_first[:, FIRST_DILATION:, :], received_head_rows], axis=1
    )
    grad_signal = (local_one + trailing_later_rows.astype(jnp.float32)).astype(jnp.bfloat16)
    reduced, grad_signal = reduce_grads(tuple(first_layer_terms) + tuple(second_layer_terms), scale_factor, grad_signal)
    reduced_one, reduced_two = reduced[:3], reduced[3:]
    return (
        grad_signal,
        reduced_one[0],
        reduced_one[1],
        reduced_one[2],
        reduced_two[0],
        reduced_two[1],
        reduced_two[2],
    )


def solution(mesh):
    in_specs = (P("dp", "tm", None), P("dp", "tm", None), P(), P(), P(), P(), P(), P())
    out_specs = (P("dp", "tm", None), P(), P(), P(), P(), P(), P())
    return jax.shard_map(body, mesh=mesh, in_specs=in_specs, out_specs=out_specs, check_vma=False)
```

```python
import math

import jax
import jax.numpy as jnp
from jax import lax
from jax.sharding import PartitionSpec as P

FIRST_DILATION = 512
SECOND_DILATION = 8192


def shifted(value, axis, steps):
    count = lax.axis_size(axis)
    leading, last = (max(0, -steps), min(count, count - steps))
    return lax.ppermute(value, axis, [(source, source + steps) for source in range(leading, last)])


def forward_layer(input_traces, past_rows, tap_past, tap_now, mixing):
    channels = input_traces.shape[-1]
    flat_now = input_traces.reshape(-1, channels)
    flat_past = past_rows.reshape(-1, channels)
    pre_act = jnp.dot(flat_past, tap_past, preferred_element_type=jnp.float32) + jnp.dot(
        flat_now, tap_now, preferred_element_type=jnp.float32
    )
    half_width = pre_act.shape[1] // 2
    filter_part = jnp.tanh(pre_act[:, :half_width])
    gate_part = jax.nn.sigmoid(pre_act[:, half_width:])
    hidden = (filter_part * gate_part).astype(jnp.bfloat16)
    output = (
        flat_now.astype(jnp.float32) + jnp.dot(hidden, mixing, preferred_element_type=jnp.float32)
    ).astype(jnp.bfloat16)
    return (filter_part, gate_part, hidden, output.reshape(input_traces.shape))


def backward_layer(input_traces, past_rows, saved, incoming_gradient, tap_past, tap_now, mixing):
    filter_part, gate_part, hidden, output = saved
    channels = input_traces.shape[-1]
    flat_now = input_traces.reshape(-1, channels)
    flat_past = past_rows.reshape(-1, channels)
    flat_up = incoming_gradient.reshape(-1, channels)
    hidden_grad = jnp.dot(flat_up, mixing.T, preferred_element_type=jnp.float32)
    filter_grad = hidden_grad * gate_part * (1.0 - filter_part * filter_part)
    gate_grad = hidden_grad * filter_part * gate_part * (1.0 - gate_part)
    pre_grad = jnp.concatenate([filter_grad, gate_grad], axis=1).astype(jnp.bfloat16)
    past_term = jnp.einsum("rc,rg->cg", flat_past, pre_grad, preferred_element_type=jnp.float32)
    now_term = jnp.einsum("rc,rg->cg", flat_now, pre_grad, preferred_element_type=jnp.float32)
    mix_term = jnp.einsum("rh,rc->hc", hidden, flat_up, preferred_element_type=jnp.float32)
    ahead_rows = (
        jnp.dot(pre_grad, tap_past.T, preferred_element_type=jnp.float32)
        .astype(jnp.bfloat16)
        .reshape(input_traces.shape)
    )
    local_grad = (
        flat_up.astype(jnp.float32)
        + jnp.dot(pre_grad, tap_now.T, preferred_element_type=jnp.float32)
    ).reshape(input_traces.shape)
    return (local_grad, ahead_rows, (past_term, now_term, mix_term))


HALVING_STEPS = ((1, 1), (32, 64), (64, 32), (2, 256), (256, 2), (128, 128))
AXES = ("dp", "tm")
BUTTERFLY_STEPS = (("tm", 4), ("tm", 8), ("tm", 16))


def paired(value, masks):
    count = lax.axis_size(AXES)
    pairs = [(source, source ^ masks[source & 1]) for source in range(count)]
    return lax.ppermute(value, AXES, pairs)


def upper_of(masks):
    index = lax.axis_index(AXES)
    return (index & jnp.where((index & 1) != 0, masks[1], masks[0])) != 0


def exchange(value, axis, mask):
    count = lax.axis_size(axis)
    return lax.ppermute(value, axis, [(source, source ^ mask) for source in range(count)])


def reduce_grads(term_list, scale_factor, companion):
    past_one, now_one, mix_one, past_two, now_two, mix_two = term_list
    blocks = (past_one, now_one, past_two, now_two, jnp.concatenate([mix_one, mix_two], axis=1))
    flat = jnp.concatenate(blocks)
    for step, masks in enumerate(HALVING_STEPS):
        half = flat.shape[0] // 2
        upper = upper_of(masks)
        first, second = flat[:half], flat[half:]
        kept = jnp.where(upper, second, first)
        sent = jnp.where(upper, first, second)
        flat = kept + paired(sent, masks)
        if step == 1:
            flat, companion = lax.optimization_barrier((flat, companion))
    for axis, mask in BUTTERFLY_STEPS:
        flat = flat + exchange(flat, axis, mask)
    flat = (flat * scale_factor).astype(jnp.bfloat16)
    for masks in reversed(HALVING_STEPS):
        upper = upper_of(masks)
        other = paired(flat, masks)
        flat = jnp.where(upper, jnp.concatenate([other, flat]), jnp.concatenate([flat, other]))
    rows = past_one.shape[0]
    parts = [flat[index * rows:(index + 1) * rows] for index in range(len(blocks))]
    mix_width = mix_one.shape[1]
    out = (parts[0], parts[1], parts[4][:, :mix_width], parts[2], parts[3], parts[4][:, mix_width:])
    return out, companion


def body(
    signal,
    cotangent,
    first_history_weight,
    first_current_weight,
    first_residual_weight,
    second_history_weight,
    second_current_weight,
    second_residual_weight,
):
    seq_count, number_of_steps, channels = signal.shape
    rows_all = seq_count * lax.axis_size("dp") * number_of_steps * lax.axis_size("tm")
    scale_factor = 1.0 / math.sqrt(rows_all)
    final_rows = signal[:, number_of_steps - FIRST_DILATION :, :]
    received_rows = shifted(final_rows, "tm", 1)
    first_history_rows = jnp.concatenate(
        [received_rows, signal[:, : number_of_steps - FIRST_DILATION, :]], axis=1
    )
    first_layer_stash = forward_layer(
        signal,
        first_history_rows,
        first_history_weight,
        first_current_weight,
        first_residual_weight,
    )
    hidden_activation = first_layer_stash[3]
    distant_offsets = SECOND_DILATION // number_of_steps
    chunk_count = 4
    chunk_rows = number_of_steps // chunk_count
    local_parts, arrived_parts, term_parts, past_parts = [], [], [], []
    for chunk in range(chunk_count):
        rows = slice(chunk * chunk_rows, (chunk + 1) * chunk_rows)
        hidden_chunk = hidden_activation[:, rows, :]
        if chunk:
            hidden_chunk, _ = lax.optimization_barrier((hidden_chunk, past_parts[-1]))
        past_chunk = shifted(hidden_chunk, "tm", distant_offsets)
        past_parts.append(past_chunk)
        chunk_stash = forward_layer(
            hidden_chunk,
            past_chunk,
            second_history_weight,
            second_current_weight,
            second_residual_weight,
        )
        local_chunk, ahead_chunk, chunk_terms = backward_layer(
            hidden_chunk,
            past_chunk,
            chunk_stash,
            cotangent[:, rows, :],
            second_history_weight,
            second_current_weight,
            second_residual_weight,
        )
        local_parts.append(local_chunk)
        arrived_parts.append(shifted(ahead_chunk, "tm", -distant_offsets))
        term_parts.append(chunk_terms)
    local_two = jnp.concatenate(local_parts, axis=1)
    arrived_back = jnp.concatenate(arrived_parts, axis=1)
    second_layer_terms = tuple(sum(members[1:], members[0]) for members in zip(*term_parts))
    hidden_gradient = (local_two + arrived_back.astype(jnp.float32)).astype(jnp.bfloat16)
    local_one, forward_rows_first, first_layer_terms = backward_layer(
        signal,
        first_history_rows,
        first_layer_stash,
        hidden_gradient,
        first_history_weight,
        first_current_weight,
        first_residual_weight,
    )
    leading_rows = forward_rows_first[:, :FIRST_DILATION, :]
    received_head_rows = shifted(leading_rows, "tm", -1)
    trailing_later_rows = jnp.concatenate(
        [forward_rows_first[:, FIRST_DILATION:, :], received_head_rows], axis=1
    )
    grad_signal = (local_one + trailing_later_rows.astype(jnp.float32)).astype(jnp.bfloat16)
    reduced, grad_signal = reduce_grads(tuple(first_layer_terms) + tuple(second_layer_terms), scale_factor, grad_signal)
    reduced_one, reduced_two = reduced[:3], reduced[3:]
    return (
        grad_signal,
        reduced_one[0],
        reduced_one[1],
        reduced_one[2],
        reduced_two[0],
        reduced_two[1],
        reduced_two[2],
    )


def solution(mesh):
    in_specs = (P("dp", "tm", None), P("dp", "tm", None), P(), P(), P(), P(), P(), P())
    out_specs = (P("dp", "tm", None), P(), P(), P(), P(), P(), P())
    return jax.shard_map(body, mesh=mesh, in_specs=in_specs, out_specs=out_specs, check_vma=False)
```
